256 devices in a mesh: section: 8 (over z), ctx: 32 (over x, y, core).
Axes of the slice: x: 4, y: 4, z: 8, core: 2. Of those that a mesh axis runs over, the one named last changes fastest.
Arguments:
- queries: bfloat16 [8, 8192, 2560], P('section', 'ctx'), may hold values from -5 to 5
- keys: bfloat16 [8, 8192, 512], P('section', 'ctx'), may hold values from -5 to 5
- values: bfloat16 [8, 8192, 512], P('section', 'ctx'), may hold values from -6 to 6
- output_cotangent: bfloat16 [8, 8192, 2560], P('section', 'ctx'), may hold values from -6 to 6
- doc_start: int32 [8, 8192], P('section', 'ctx'), may hold values from 0 to 8191, as said below
Outputs:
- attn: bfloat16 [8, 8192, 2560], P('section', 'ctx')
- handed_dq: bfloat16 [8, 8192, 2560], P('section', 'ctx')
- handed_kv: bfloat16 [8, 2, 8192, 512], P('section', None, 'ctx')
The draws below stay inside these ranges and needn't reach their ends.
Inputs may be any that keep to these rules, and one draw needn't show every extreme that they name: doc_start[m, i] is the first position of the document holding token i; documents are 768 tokens long at most, every microbatch holds one of exactly 768 tokens, and its last token is a document of its own.
All inputs are finite; a program needn't handle non-finite values.
Results may differ from the reference program's by a relative error of at most 0.012.
The reference program's roundings to bfloat16 on the way (of `prob_b`, `dscore` and `grad_q`) count: a program that leaves them out, or rounds other values in their place, can miss the bound.
Values may be sent and summed in bfloat16 or wider, within the bound.
No kernel may reach another device: no remote copies, remote signals or barrier semaphores. Data moves between devices by JAX's collectives and lax.ppermute only.
A program may use at most 64 MiB of HBM per device.

```python
import jax
import jax.numpy as jnp
from jax import lax

QUERY_HEADS = 20
KEY_VALUE_HEADS = 4
HEAD_WIDTH = 128
REACH = 3
TOK_DEV = 256
QUERY_PER_KV = 5
TOKEN_LENGTH = 8192
MICROBATCH_COUNT = 8
MOST = 768
N_CTX = 32


def drawn_pair(key):
    base = jax.random.fold_in(key, 1234)
    key_q, key_k = jax.random.split(base, 2)
    query_shape = (MICROBATCH_COUNT, TOKEN_LENGTH, QUERY_HEADS * HEAD_WIDTH)
    key_shape = (MICROBATCH_COUNT, TOKEN_LENGTH, KEY_VALUE_HEADS * HEAD_WIDTH)
    queries_out = jnp.clip(jax.random.normal(key_q, query_shape, jnp.float32), -4.0, 4.0)
    keys_out = jnp.clip(jax.random.normal(key_k, key_shape, jnp.float32), -4.0, 4.0)
    return (queries_out, keys_out)


def draw_queries(key, part):
    return drawn_pair(key)[0].astype(jnp.bfloat16)


def draw_keys(key, part):
    return drawn_pair(key)[1].astype(jnp.bfloat16)


def draw_doc_start(key, part):
    base = jax.random.fold_in(key, 99)
    keys_all = jax.random.split(base, MICROBATCH_COUNT)
    lower = max(1, MOST // 64)
    upper = max(lower + 1, MOST // 8)

    def single(subkey):
        key_a, key_b, key_c = jax.random.split(subkey, 3)
        short = jax.random.randint(key_a, (TOKEN_LENGTH,), lower, upper)
        longer = jax.random.randint(key_b, (TOKEN_LENGTH,), upper, MOST + 1)
        chosen = jax.random.randint(key_c, (TOKEN_LENGTH,), 0, 4) == 0
        lengths = jnp.where(chosen, longer, short)
        lengths = lengths.at[0].set(short[0]).at[1].set(MOST)
        ends = jnp.cumsum(lengths).astype(jnp.int32)
        rows = jnp.arange(TOKEN_LENGTH, dtype=jnp.int32)
        index = jnp.searchsorted(ends, rows, side='right')
        begins = jnp.concatenate([jnp.zeros((1,), jnp.int32), ends[:-1]])
        result = begins[index].astype(jnp.int32)
        return result.at[TOKEN_LENGTH - 1].set(TOKEN_LENGTH - 1)
    return jax.vmap(single)(keys_all)


def level_of(own_key, shape, cuts, least, high):
    factor_of, own = 1.0, jax.random.fold_in(own_key, 6)
    for dim, blocks in cuts:
        draws = jnp.exp(jax.random.uniform(jax.random.fold_in(own, dim), (blocks,), jnp.float32, least / len(cuts), high / len(cuts)))
        factor_of = factor_of * jnp.repeat(draws, shape[dim] // blocks).reshape([-1 if axis == dim else 1 for axis in range(len(shape))])
    return factor_of


def centred(stream_key, shape, width, limit, pieces=(), kind=jnp.bfloat16):
    array = width * jax.random.normal(stream_key, shape, jnp.float32)
    if pieces:
        array = array * level_of(stream_key, shape, pieces, -0.22, 0.18)
    return jnp.clip(array, -limit, limit).astype(kind)


def setup_inputs(seed: int = 0) -> dict:
    seeds = jax.random.split(jax.random.key(seed), 6)
    return {
        "queries": draw_queries(jax.random.fold_in(seeds[5], 71), 0),
        "keys": draw_keys(jax.random.fold_in(seeds[5], 71), 0),
        "values": centred(seeds[2], (MICROBATCH_COUNT, TOKEN_LENGTH, KEY_VALUE_HEADS * HEAD_WIDTH), 1.0, 6.0, ((0, 8), (1, 32))),
        "output_cotangent": centred(seeds[3], (MICROBATCH_COUNT, TOKEN_LENGTH, QUERY_HEADS * HEAD_WIDTH), 1.0, 6.0, ((0, 8), (1, 32))),
        "doc_start": draw_doc_start(jax.random.fold_in(seeds[5], 71), 0),
    }


def group_terms(query_part, dout_part, key_part, value_part, visible, scale):
    query_f = query_part.astype(jnp.float32)
    dout_f = dout_part.astype(jnp.float32)
    key_f = key_part.astype(jnp.float32)
    value_f = value_part.astype(jnp.float32)
    scores = jnp.einsum("tgd,wd->gtw", query_f, key_f) * scale
    scores = jnp.where(visible[None], scores, -jnp.inf)
    top = jnp.max(scores, axis=-1, keepdims=True)
    total = jnp.sum(jnp.exp(scores - top), axis=-1, keepdims=True)
    lse = top + jnp.log(total)
    prob = jnp.exp(scores - lse)
    prob_b = lax.optimization_barrier(prob.astype(jnp.bfloat16)).astype(jnp.float32)
    attn = jnp.einsum("gtw,wd->tgd", prob_b, value_f).astype(jnp.bfloat16)
    attn_f = lax.optimization_barrier(attn).astype(jnp.float32)
    delta = jnp.sum(dout_f * attn_f, axis=-1)
    dprob = jnp.einsum("tgd,wd->gtw", dout_f, value_f)
    dscore = (prob * (dprob - jnp.transpose(delta)[:, :, None]) * scale).astype(jnp.bfloat16)
    dscore_f = lax.optimization_barrier(dscore).astype(jnp.float32)
    grad_q = jnp.einsum("gtw,wd->tgd", dscore_f, key_f).astype(jnp.bfloat16)
    key_gradient = jnp.einsum("gtw,tgd->wd", dscore_f, query_f)
    value_gradient = jnp.einsum("gtw,tgd->wd", prob_b, dout_f)
    return attn, grad_q, key_gradient, value_gradient


def microbatch(parts):
    queries, keys, values, output_cotangent, doc_start = parts
    local_tokens = TOK_DEV
    token_span = (REACH + 1) * local_tokens
    leading_rows = REACH * local_tokens
    scale = HEAD_WIDTH ** -0.5
    paired_rows = jnp.stack([keys, values])
    padded_rows = jnp.concatenate([jnp.zeros((2, leading_rows, KEY_VALUE_HEADS * HEAD_WIDTH), paired_rows.dtype), paired_rows], axis=1)

    def step(accum, block):
        leading_entry = (block * local_tokens).astype(jnp.int32)
        query_matrix = lax.dynamic_slice_in_dim(queries, leading_entry, local_tokens, 0).reshape(local_tokens, KEY_VALUE_HEADS, QUERY_PER_KV, HEAD_WIDTH)
        output_grad_rows = lax.dynamic_slice_in_dim(output_cotangent, leading_entry, local_tokens, 0).reshape(local_tokens, KEY_VALUE_HEADS, QUERY_PER_KV, HEAD_WIDTH)
        starts = lax.dynamic_slice_in_dim(doc_start, leading_entry, local_tokens, 0)
        attention_window = lax.dynamic_slice_in_dim(padded_rows, leading_entry, token_span, 1).reshape(2, token_span, KEY_VALUE_HEADS, HEAD_WIDTH)
        query_pos = leading_entry + jnp.arange(local_tokens, dtype=jnp.int32)
        key_pos = leading_entry - leading_rows + jnp.arange(token_span, dtype=jnp.int32)
        visible = (key_pos[None, :] >= starts[:, None]) & (key_pos[None, :] <= query_pos[:, None])

        def per_group(items):
            return group_terms(items[0], items[1], items[2], items[3], visible, scale)

        attn, grad_q, key_gradient, value_gradient = lax.map(per_group, (jnp.moveaxis(query_matrix, 1, 0), jnp.moveaxis(output_grad_rows, 1, 0), jnp.moveaxis(attention_window[0], 1, 0), jnp.moveaxis(attention_window[1], 1, 0)))
        attn_rows = jnp.moveaxis(attn, 0, 1).reshape(local_tokens, QUERY_HEADS * HEAD_WIDTH)
        grad_q_rows = jnp.moveaxis(grad_q, 0, 1).reshape(local_tokens, QUERY_HEADS * HEAD_WIDTH)
        key_value_gradient = jnp.stack([jnp.moveaxis(key_gradient, 0, 1).reshape(token_span, KEY_VALUE_HEADS * HEAD_WIDTH), jnp.moveaxis(value_gradient, 0, 1).reshape(token_span, KEY_VALUE_HEADS * HEAD_WIDTH)])
        current = lax.dynamic_slice_in_dim(accum, leading_entry, token_span, 1)
        accum = lax.dynamic_update_slice_in_dim(accum, current + key_value_gradient, leading_entry, 1)
        return accum, (attn_rows, grad_q_rows)

    initial_accumulator = jnp.zeros((2, leading_rows + TOKEN_LENGTH, KEY_VALUE_HEADS * HEAD_WIDTH), jnp.float32)
    accum, (attn, grad_q) = lax.scan(step, initial_accumulator, jnp.arange(N_CTX, dtype=jnp.int32))
    return attn.reshape(TOKEN_LENGTH, QUERY_HEADS * HEAD_WIDTH), grad_q.reshape(TOKEN_LENGTH, QUERY_HEADS * HEAD_WIDTH), accum[:, leading_rows:].astype(jnp.bfloat16)


def reference(queries, keys, values, output_cotangent, doc_start):
    attn, grad_q, key_value_gradient = lax.map(microbatch, (queries, keys, values, output_cotangent, doc_start))
    handed_dq = jnp.concatenate([grad_q[1:], jnp.zeros_like(grad_q[:1])], axis=0)
    handed_kv = jnp.concatenate([key_value_gradient[1:], jnp.zeros_like(key_value_gradient[:1])], axis=0)
    return attn, handed_dq, handed_kv
```

```python
import functools

import jax
import jax.numpy as jnp
from jax import lax
from jax.experimental import pallas as pl
from jax.experimental.pallas import tpu as pltpu
from jax.sharding import PartitionSpec as P

HEAD_WIDTH = 128
REACH = 3


def shifted(value, axis, steps):
    count = lax.axis_size(axis)
    first, last = (max(0, -steps), min(count, count - steps))
    return lax.ppermute(value, axis, [(source, source + steps) for source in range(first, last)])


def head_kernel(starts_ref, q_ref, do_ref, k_ref, v_ref, attn_ref, gq_ref, gk_ref, gv_ref, *, scale):
    head = pl.program_id(1)
    q = q_ref[...]
    do = do_ref[...]
    k = k_ref[...]
    v = v_ref[...]
    rows, span = q.shape[0], k.shape[0]
    scores = lax.dot_general(q, k, (((1,), (1,)), ((), ())), preferred_element_type=jnp.float32) * scale
    row = lax.broadcasted_iota(jnp.int32, (rows, span), 0)
    col = lax.broadcasted_iota(jnp.int32, (rows, span), 1)
    visible = (col >= starts_ref[...]) & (col <= row + (span - rows))
    scores = jnp.where(visible, scores, -jnp.inf)
    top = jnp.max(scores, axis=1, keepdims=True)
    total = jnp.sum(jnp.exp(scores - top), axis=1, keepdims=True)
    lse = top + jnp.log(total)
    prob = jnp.exp(scores - lse)
    prob_b = prob.astype(jnp.bfloat16)
    attn = jnp.dot(prob_b, v, preferred_element_type=jnp.float32).astype(jnp.bfloat16)
    attn_ref[...] = attn
    delta = jnp.sum(do.astype(jnp.float32) * attn.astype(jnp.float32), axis=1, keepdims=True)
    dprob = lax.dot_general(do, v, (((1,), (1,)), ((), ())), preferred_element_type=jnp.float32)
    dscore = (prob * (dprob - delta) * scale).astype(jnp.bfloat16)
    gq_ref[...] = jnp.dot(dscore, k, preferred_element_type=jnp.float32).astype(jnp.bfloat16)
    gk = lax.dot_general(dscore, q, (((0,), (0,)), ((), ())), preferred_element_type=jnp.float32)
    gv = lax.dot_general(prob_b, do, (((0,), (0,)), ((), ())), preferred_element_type=jnp.float32)

    @pl.when(head == 0)
    def _():
        gk_ref[...] = gk
        gv_ref[...] = gv

    @pl.when(head > 0)
    def _():
        gk_ref[...] += gk
        gv_ref[...] += gv


def attention_terms(rel_starts, queries, dout, window_k, window_v, heads_kv, group_size):
    rows = queries.shape[0]
    span = window_k.shape[0]
    scale = HEAD_WIDTH ** (-0.5)
    kernel = functools.partial(head_kernel, scale=scale)
    q_spec = pl.BlockSpec((rows, HEAD_WIDTH), lambda g, h: (0, g * group_size + h))
    kv_spec = pl.BlockSpec((span, HEAD_WIDTH), lambda g, h: (0, g))
    return pl.pallas_call(
        kernel,
        grid=(heads_kv, group_size),
        in_specs=[
            pl.BlockSpec((rows, 1), lambda g, h: (0, 0)),
            q_spec,
            q_spec,
            kv_spec,
            kv_spec,
        ],
        out_specs=[q_spec, q_spec, kv_spec, kv_spec],
        out_shape=[
            jax.ShapeDtypeStruct(queries.shape, jnp.bfloat16),
            jax.ShapeDtypeStruct(queries.shape, jnp.bfloat16),
            jax.ShapeDtypeStruct(window_k.shape, jnp.float32),
            jax.ShapeDtypeStruct(window_k.shape, jnp.float32),
        ],
        compiler_params=pltpu.CompilerParams(
            dimension_semantics=("arbitrary", "arbitrary"),
            vmem_limit_bytes=48 * 1024 * 1024,
        ),
    )(rel_starts, queries, dout, window_k, window_v)


def local(queries, keys, values, output_cotangent, doc_start):
    local_tokens = queries.shape[1]
    heads_kv = keys.shape[2] // HEAD_WIDTH
    group_size = queries.shape[2] // keys.shape[2]
    position = lax.axis_index("ctx")
    leading_entry = position * local_tokens
    window_base = leading_entry - REACH * local_tokens
    rel_starts = (doc_start[0] - window_base).astype(jnp.int32)[:, None]
    own_block = jnp.stack([keys[0], values[0]])
    earlier = [shifted(own_block, "ctx", stride) for stride in range(1, REACH + 1)]
    window = jnp.concatenate(earlier[::-1] + [own_block], axis=1)
    attn, grad_q, grad_k, grad_v = attention_terms(
        rel_starts, queries[0], output_cotangent[0], window[0], window[1], heads_kv, group_size
    )
    partial_terms = jnp.stack([grad_k, grad_v])

    def owner_piece(behind):
        offset = (REACH - behind) * local_tokens
        return partial_terms[:, offset : offset + local_tokens]

    summed = owner_piece(0)
    for behind in range(1, REACH + 1):
        piece = owner_piece(behind).astype(jnp.bfloat16)
        summed = summed + shifted(piece, "ctx", -behind).astype(jnp.float32)
    kv_grads = summed.astype(jnp.bfloat16)
    handed_dq, handed_kv = shifted((grad_q[None], kv_grads[None]), "section", -1)
    return (attn[None], handed_dq, handed_kv)


def solution(mesh):
    return jax.shard_map(
        local,
        mesh=mesh,
        in_specs=(
            P("section", "ctx", None),
            P("section", "ctx", None),
            P("section", "ctx", None),
            P("section", "ctx", None),
            P("section", "ctx"),
        ),
        out_specs=(
            P("section", "ctx", None),
            P("section", "ctx", None),
            P("section", None, "ctx", None),
        ),
        check_vma=False,
    )
```

```python
import functools

import jax
import jax.numpy as jnp
from jax import lax
from jax.experimental import pallas as pl
from jax.experimental.pallas import tpu as pltpu
from jax.sharding import PartitionSpec as P

HEAD_WIDTH = 128
REACH = 3


def shifted(value, axis, steps):
    count = lax.axis_size(axis)
    first, last = (max(0, -steps), min(count, count - steps))
    return lax.ppermute(value, axis, [(source, source + steps) for source in range(first, last)])


def head_kernel(starts_ref, q_ref, do_ref, k_ref, v_ref, attn_ref, gq_ref, gk_ref, gv_ref, *, scale):
    head = pl.program_id(0)
    q = q_ref[...]
    do = do_ref[...]
    k = k_ref[...]
    v = v_ref[...]
    rows, span = q.shape[0], k.shape[0]
    scores = lax.dot_general(q, k, (((1,), (1,)), ((), ())), preferred_element_type=jnp.float32) * scale
    row = lax.broadcasted_iota(jnp.int32, (rows, span), 0)
    col = lax.broadcasted_iota(jnp.int32, (rows, span), 1)
    visible = (col >= starts_ref[...]) & (col <= row + (span - rows))
    scores = jnp.where(visible, scores, -jnp.inf)
    top = jnp.max(scores, axis=1, keepdims=True)
    total = jnp.sum(jnp.exp(scores - top), axis=1, keepdims=True)
    lse = top + jnp.log(total)
    prob = jnp.exp(scores - lse)
    prob_b = prob.astype(jnp.bfloat16)
    attn = jnp.dot(prob_b, v, preferred_element_type=jnp.float32).astype(jnp.bfloat16)
    attn_ref[...] = attn
    delta = jnp.sum(do.astype(jnp.float32) * attn.astype(jnp.float32), axis=1, keepdims=True)
    dprob = lax.dot_general(do, v, (((1,), (1,)), ((), ())), preferred_element_type=jnp.float32)
    dscore = (prob * (dprob - delta) * scale).astype(jnp.bfloat16)
    gq_ref[...] = jnp.dot(dscore, k, preferred_element_type=jnp.float32).astype(jnp.bfloat16)
    gk = lax.dot_general(dscore, q, (((0,), (0,)), ((), ())), preferred_element_type=jnp.float32)
    gv = lax.dot_general(prob_b, do, (((0,), (0,)), ((), ())), preferred_element_type=jnp.float32)

    @pl.when(head == 0)
    def _():
        gk_ref[...] = gk
        gv_ref[...] = gv

    @pl.when(head > 0)
    def _():
        gk_ref[...] += gk
        gv_ref[...] += gv


def group_terms(rel_starts, queries, dout, window_k, window_v, group, group_size):
    rows = queries.shape[0]
    span = window_k.shape[0]
    scale = HEAD_WIDTH ** (-0.5)
    kernel = functools.partial(head_kernel, scale=scale)
    q_spec = pl.BlockSpec((rows, HEAD_WIDTH), lambda h: (0, group * group_size + h))
    out_spec = pl.BlockSpec((rows, HEAD_WIDTH), lambda h: (0, h))
    kv_spec = pl.BlockSpec((span, HEAD_WIDTH), lambda h: (0, 0))
    group_shape = (rows, group_size * HEAD_WIDTH)
    return pl.pallas_call(
        kernel,
        grid=(group_size,),
        in_specs=[pl.BlockSpec((rows, 1), lambda h: (0, 0)), q_spec, q_spec, kv_spec, kv_spec],
        out_specs=[out_spec, out_spec, kv_spec, kv_spec],
        out_shape=[
            jax.ShapeDtypeStruct(group_shape, jnp.bfloat16),
            jax.ShapeDtypeStruct(group_shape, jnp.bfloat16),
            jax.ShapeDtypeStruct(window_k.shape, jnp.float32),
            jax.ShapeDtypeStruct(window_k.shape, jnp.float32),
        ],
        compiler_params=pltpu.CompilerParams(
            dimension_semantics=("arbitrary",),
            vmem_limit_bytes=48 * 1024 * 1024,
        ),
    )(rel_starts, queries, dout, window_k, window_v)


def moved(value, pairs):
    return lax.ppermute(value, "ctx", pairs)


def earlier_blocks(own, count, even):
    two_back = moved(own, [(d, d + 2) for d in range(count - 2)])
    partner_own = moved(own, [(d, d + 1) for d in range(0, count, 2)])
    partner_two = moved(two_back, [(d, d + 1) for d in range(0, count, 2)])
    odd_two = moved(two_back, [(d + 1, d) for d in range(0, count, 2)])
    relay = moved(two_back, [(d, d + 1) for d in range(1, count - 1, 2)])
    three_back = jnp.where(even, relay, partner_two)
    one_back = jnp.where(even, odd_two, partner_own)
    return three_back, two_back, one_back


def returned_terms(terms, rows, count, pending):
    piece = [terms[:, index * rows : (index + 1) * rows] for index in range(REACH + 1)]
    back3 = piece[0].astype(jnp.bfloat16)
    back1 = piece[2].astype(jnp.bfloat16)
    relay = moved(back3, [(d, d - 1) for d in range(2, count, 2)])
    to_even = moved(jnp.stack([back1, back3]), [(d + 1, d) for d in range(0, count, 2)])
    to_odd = moved(back1, [(d, d + 1) for d in range(0, count, 2)])
    pending.extend([relay, to_even, to_odd])
    gathered = (
        piece[1]
        + relay.astype(jnp.float32)
        + to_odd.astype(jnp.float32)
        + to_even[1].astype(jnp.float32)
    )
    far = moved(gathered.astype(jnp.bfloat16), [(d, d - 2) for d in range(2, count)])
    total = piece[3] + to_even[0].astype(jnp.float32) + far.astype(jnp.float32)
    return total.astype(jnp.bfloat16)


def local(queries, keys, values, output_cotangent, doc_start):
    local_tokens = queries.shape[1]
    heads_kv = keys.shape[2] // HEAD_WIDTH
    group_size = queries.shape[2] // keys.shape[2]
    count = lax.axis_size("ctx")
    position = lax.axis_index("ctx")
    even = position % 2 == 0
    leading_entry = position * local_tokens
    window_base = leading_entry - REACH * local_tokens
    rel_starts = (doc_start[0] - window_base).astype(jnp.int32)[:, None]
    attn_parts, dq_parts, kv_parts = [], [], []
    pending = [[] for _ in range(heads_kv + 2)]
    for group in range(heads_kv):
        columns = slice(group * HEAD_WIDTH, (group + 1) * HEAD_WIDTH)
        own = jnp.stack([keys[0][:, columns], values[0][:, columns]])
        three_back, two_back, one_back = earlier_blocks(own, count, even)
        window = jnp.concatenate([three_back, two_back, one_back, own], axis=1)
        group_starts = rel_starts
        if pending[group]:
            group_starts, _ = lax.optimization_barrier((rel_starts, pending[group]))
        attn, grad_q, grad_k, grad_v = group_terms(
            group_starts, queries[0], output_cotangent[0], window[0], window[1], group, group_size
        )
        kv_grads = returned_terms(jnp.stack([grad_k, grad_v]), local_tokens, count, pending[group + 2])
        dq_parts.append(shifted(grad_q[None], "section", -1))
        pending[group + 2].append(dq_parts[-1])
        kv_parts.append(shifted(kv_grads[None], "section", -1))
        attn_parts.append(attn)
    attn = jnp.concatenate(attn_parts, axis=1)
    handed_dq = jnp.concatenate(dq_parts, axis=2)
    handed_kv = jnp.concatenate(kv_parts, axis=3)
    return (attn[None], handed_dq, handed_kv)


def solution(mesh):
    return jax.shard_map(
        local,
        mesh=mesh,
        in_specs=(
            P("section", "ctx", None),
            P("section", "ctx", None),
            P("section", "ctx", None),
            P("section", "ctx", None),
            P("section", "ctx"),
        ),
        out_specs=(
            P("section", "ctx", None),
            P("section", "ctx", None),
            P("section", None, "ctx", None),
        ),
        check_vma=False,
    )
```

```python
import functools

import jax
import jax.numpy as jnp
from jax import lax
from jax.experimental import pallas as pl
from jax.experimental.pallas import tpu as pltpu
from jax.sharding import PartitionSpec as P

HEAD_WIDTH = 128
REACH = 3


def shifted(value, axis, steps):
    count = lax.axis_size(axis)
    first, last = (max(0, -steps), min(count, count - steps))
    return lax.ppermute(value, axis, [(source, source + steps) for source in range(first, last)])


def head_kernel(starts_ref, q_ref, do_ref, k_ref, v_ref, attn_ref, gq_ref, gk_ref, gv_ref, *, scale):
    head = pl.program_id(1)
    q = q_ref[...]
    do = do_ref[...]
    k = k_ref[...]
    v = v_ref[...]
    rows, span = q.shape[0], k.shape[0]
    scores = lax.dot_general(q, k, (((1,), (1,)), ((), ())), preferred_element_type=jnp.float32) * scale
    row = lax.broadcasted_iota(jnp.int32, (rows, span), 0)
    col = lax.broadcasted_iota(jnp.int32, (rows, span), 1)
    visible = (col >= starts_ref[...]) & (col <= row + (span - rows))
    scores = jnp.where(visible, scores, -jnp.inf)
    top = jnp.max(scores, axis=1, keepdims=True)
    total = jnp.sum(jnp.exp(scores - top), axis=1, keepdims=True)
    lse = top + jnp.log(total)
    prob = jnp.exp(scores - lse)
    prob_b = prob.astype(jnp.bfloat16)
    attn = jnp.dot(prob_b, v, preferred_element_type=jnp.float32).astype(jnp.bfloat16)
    attn_ref[...] = attn
    delta = jnp.sum(do.astype(jnp.float32) * attn.astype(jnp.float32), axis=1, keepdims=True)
    dprob = lax.dot_general(do, v, (((1,), (1,)), ((), ())), preferred_element_type=jnp.float32)
    dscore = (prob * (dprob - delta) * scale).astype(jnp.bfloat16)
    gq_ref[...] = jnp.dot(dscore, k, preferred_element_type=jnp.float32).astype(jnp.bfloat16)
    gk = lax.dot_general(dscore, q, (((0,), (0,)), ((), ())), preferred_element_type=jnp.float32)
    gv = lax.dot_general(prob_b, do, (((0,), (0,)), ((), ())), preferred_element_type=jnp.float32)

    @pl.when(head == 0)
    def _():
        gk_ref[...] = gk
        gv_ref[...] = gv

    @pl.when(head > 0)
    def _():
        gk_ref[...] += gk
        gv_ref[...] += gv


def attention_terms(rel_starts, queries, dout, window_k, window_v, heads_kv, group_size):
    rows = queries.shape[0]
    span = window_k.shape[0]
    scale = HEAD_WIDTH ** (-0.5)
    kernel = functools.partial(head_kernel, scale=scale)
    q_spec = pl.BlockSpec((rows, HEAD_WIDTH), lambda g, h: (0, g * group_size + h))
    kv_spec = pl.BlockSpec((span, HEAD_WIDTH), lambda g, h: (0, g))
    return pl.pallas_call(
        kernel,
        grid=(heads_kv, group_size),
        in_specs=[
            pl.BlockSpec((rows, 1), lambda g, h: (0, 0)),
            q_spec,
            q_spec,
            kv_spec,
            kv_spec,
        ],
        out_specs=[q_spec, q_spec, kv_spec, kv_spec],
        out_shape=[
            jax.ShapeDtypeStruct(queries.shape, jnp.bfloat16),
            jax.ShapeDtypeStruct(queries.shape, jnp.bfloat16),
            jax.ShapeDtypeStruct(window_k.shape, jnp.float32),
            jax.ShapeDtypeStruct(window_k.shape, jnp.float32),
        ],
        compiler_params=pltpu.CompilerParams(
            dimension_semantics=("arbitrary", "arbitrary"),
            vmem_limit_bytes=48 * 1024 * 1024,
        ),
    )(rel_starts, queries, dout, window_k, window_v)


def moved(value, steps):
    count = lax.axis_size("ctx")
    return lax.ppermute(value, "ctx", [(d, d + steps) for d in range(count) if 0 <= d + steps < count])


def earlier_blocks(own):
    two_back = moved(own, 2)
    pair = moved(jnp.stack([own, two_back]), 1)
    return pair[1], two_back, pair[0]


def returned_terms(terms, rows):
    piece = [terms[:, index * rows : (index + 1) * rows] for index in range(REACH + 1)]
    pair = moved(jnp.stack([piece[2], piece[0]]).astype(jnp.bfloat16), -1)
    gathered = piece[1] + pair[1].astype(jnp.float32)
    far = moved(gathered.astype(jnp.bfloat16), -2)
    total = piece[3] + pair[0].astype(jnp.float32) + far.astype(jnp.float32)
    return total.astype(jnp.bfloat16)


def local(queries, keys, values, output_cotangent, doc_start):
    local_tokens = queries.shape[1]
    heads_kv = keys.shape[2] // HEAD_WIDTH
    group_size = queries.shape[2] // keys.shape[2]
    position = lax.axis_index("ctx")
    leading_entry = position * local_tokens
    window_base = leading_entry - REACH * local_tokens
    rel_starts = (doc_start[0] - window_base).astype(jnp.int32)[:, None]
    own_block = jnp.stack([keys[0], values[0]])
    three_back, two_back, one_back = earlier_blocks(own_block)
    window = jnp.concatenate([three_back, two_back, one_back, own_block], axis=1)
    attn, grad_q, grad_k, grad_v = attention_terms(
        rel_starts, queries[0], output_cotangent[0], window[0], window[1], heads_kv, group_size
    )
    handed_dq = shifted(grad_q[None], "section", -1)
    kv_grads = returned_terms(jnp.stack([grad_k, grad_v]), local_tokens)
    handed_kv = shifted(kv_grads[None], "section", -1)
    return (attn[None], handed_dq, handed_kv)


def solution(mesh):
    return jax.shard_map(
        local,
        mesh=mesh,
        in_specs=(
            P("section", "ctx", None),
            P("section", "ctx", None),
            P("section", "ctx", None),
            P("section", "ctx", None),
            P("section", "ctx"),
        ),
        out_specs=(
            P("section", "ctx", None),
            P("section", "ctx", None),
            P("section", None, "ctx", None),
        ),
        check_vma=False,
    )
```

```python
import functools

import jax
import jax.numpy as jnp
from jax import lax
from jax.experimental import pallas as pl
from jax.experimental.pallas import tpu as pltpu
from jax.sharding import PartitionSpec as P

HEAD_WIDTH = 128
REACH = 3


def shifted(value, axis, steps):
    count = lax.axis_size(axis)
    first, last = (max(0, -steps), min(count, count - steps))
    return lax.ppermute(value, axis, [(source, source + steps) for source in range(first, last)])


def head_kernel(starts_ref, q_ref, do_ref, k_ref, v_ref, attn_ref, gq_ref, gk_ref, gv_ref, *, scale):
    head = pl.program_id(1)
    q = q_ref[...]
    do = do_ref[...]
    k = k_ref[...]
    v = v_ref[...]
    rows, span = q.shape[0], k.shape[0]
    scores = lax.dot_general(q, k, (((1,), (1,)), ((), ())), preferred_element_type=jnp.float32) * scale
    row = lax.broadcasted_iota(jnp.int32, (rows, span), 0)
    col = lax.broadcasted_iota(jnp.int32, (rows, span), 1)
    visible = (col >= starts_ref[...]) & (col <= row + (span - rows))
    scores = jnp.where(visible, scores, -jnp.inf)
    top = jnp.max(scores, axis=1, keepdims=True)
    total = jnp.sum(jnp.exp(scores - top), axis=1, keepdims=True)
    lse = top + jnp.log(total)
    prob = jnp.exp(scores - lse)
    prob_b = prob.astype(jnp.bfloat16)
    attn = jnp.dot(prob_b, v, preferred_element_type=jnp.float32).astype(jnp.bfloat16)
    attn_ref[...] = attn
    delta = jnp.sum(do.astype(jnp.float32) * attn.astype(jnp.float32), axis=1, keepdims=True)
    dprob = lax.dot_general(do, v, (((1,), (1,)), ((), ())), preferred_element_type=jnp.float32)
    dscore = (prob * (dprob - delta) * scale).astype(jnp.bfloat16)
    gq_ref[...] = jnp.dot(dscore, k, preferred_element_type=jnp.float32).astype(jnp.bfloat16)
    gk = lax.dot_general(dscore, q, (((0,), (0,)), ((), ())), preferred_element_type=jnp.float32)
    gv = lax.dot_general(prob_b, do, (((0,), (0,)), ((), ())), preferred_element_type=jnp.float32)

    @pl.when(head == 0)
    def _():
        gk_ref[...] = gk
        gv_ref[...] = gv

    @pl.when(head > 0)
    def _():
        gk_ref[...] += gk
        gv_ref[...] += gv


def attention_terms(rel_starts, queries, dout, window_k, window_v, first_group, group_size):
    rows = queries.shape[0]
    span, width = window_k.shape
    groups = width // HEAD_WIDTH
    scale = HEAD_WIDTH ** (-0.5)
    kernel = functools.partial(head_kernel, scale=scale)
    q_spec = pl.BlockSpec((rows, HEAD_WIDTH), lambda g, h: (0, (first_group + g) * group_size + h))
    out_spec = pl.BlockSpec((rows, HEAD_WIDTH), lambda g, h: (0, g * group_size + h))
    kv_spec = pl.BlockSpec((span, HEAD_WIDTH), lambda g, h: (0, g))
    out_shape = (rows, groups * group_size * HEAD_WIDTH)
    heads = groups * group_size
    cost = pl.CostEstimate(
        flops=heads * 6 * 2 * rows * span * HEAD_WIDTH,
        transcendentals=heads * 2 * rows * span,
        bytes_accessed=heads * 4 * rows * HEAD_WIDTH * 2 + groups * 2 * span * HEAD_WIDTH * 6,
    )
    return pl.pallas_call(
        kernel,
        grid=(groups, group_size),
        in_specs=[
            pl.BlockSpec((rows, 1), lambda g, h: (0, 0)),
            q_spec,
            q_spec,
            kv_spec,
            kv_spec,
        ],
        out_specs=[out_spec, out_spec, kv_spec, kv_spec],
        out_shape=[
            jax.ShapeDtypeStruct(out_shape, jnp.bfloat16),
            jax.ShapeDtypeStruct(out_shape, jnp.bfloat16),
            jax.ShapeDtypeStruct(window_k.shape, jnp.float32),
            jax.ShapeDtypeStruct(window_k.shape, jnp.float32),
        ],
        compiler_params=pltpu.CompilerParams(
            dimension_semantics=("arbitrary", "arbitrary"),
            vmem_limit_bytes=48 * 1024 * 1024,
        ),
        cost_estimate=cost,
    )(rel_starts, queries, dout, window_k, window_v)


def moved(value, steps):
    count = lax.axis_size("ctx")
    return lax.ppermute(value, "ctx", [(d, d + steps) for d in range(count) if 0 <= d + steps < count])


def earlier_blocks(own):
    two_back = moved(own, 2)
    pair = moved(jnp.stack([own, two_back]), 1)
    return pair[1], two_back, pair[0]


def returned_terms(terms, rows):
    piece = [terms[:, index * rows : (index + 1) * rows] for index in range(REACH + 1)]
    pair = moved(jnp.stack([piece[2], piece[0]]).astype(jnp.bfloat16), -1)
    gathered = piece[1] + pair[1].astype(jnp.float32)
    far = moved(gathered.astype(jnp.bfloat16), -2)
    total = piece[3] + pair[0].astype(jnp.float32) + far.astype(jnp.float32)
    return total.astype(jnp.bfloat16)


def local(queries, keys, values, output_cotangent, doc_start):
    local_tokens = queries.shape[1]
    heads_kv = keys.shape[2] // HEAD_WIDTH
    group_size = queries.shape[2] // keys.shape[2]
    position = lax.axis_index("ctx")
    leading_entry = position * local_tokens
    window_base = leading_entry - REACH * local_tokens
    rel_starts = (doc_start[0] - window_base).astype(jnp.int32)[:, None]
    halves = 2
    half_groups = heads_kv // halves
    attn_parts, dq_parts, kv_parts = [], [], []
    for half in range(halves):
        columns = slice(half * half_groups * HEAD_WIDTH, (half + 1) * half_groups * HEAD_WIDTH)
        own_block = jnp.stack([keys[0][:, columns], values[0][:, columns]])
        three_back, two_back, one_back = earlier_blocks(own_block)
        window = jnp.concatenate([three_back, two_back, one_back, own_block], axis=1)
        attn, grad_q, grad_k, grad_v = attention_terms(
            rel_starts,
            queries[0],
            output_cotangent[0],
            window[0],
            window[1],
            half * half_groups,
            group_size,
        )
        attn_parts.append(attn)
        dq_parts.append(shifted(grad_q[None], "section", -1))
        terms = jnp.stack([grad_k, grad_v])
        if half > 0:
            terms, _ = lax.optimization_barrier((terms, dq_parts[-2]))
        kv_grads = returned_terms(terms, local_tokens)
        kv_parts.append(shifted(kv_grads[None], "section", -1))
    attn = jnp.concatenate(attn_parts, axis=1)
    handed_dq = jnp.concatenate(dq_parts, axis=2)
    handed_kv = jnp.concatenate(kv_parts, axis=3)
    return (attn[None], handed_dq, handed_kv)


def solution(mesh):
    return jax.shard_map(
        local,
        mesh=mesh,
        in_specs=(
            P("section", "ctx", None),
            P("section", "ctx", None),
            P("section", "ctx", None),
            P("section", "ctx", None),
            P("section", "ctx"),
        ),
        out_specs=(
            P("section", "ctx", None),
            P("section", "ctx", None),
            P("section", None, "ctx", None),
        ),
        check_vma=False,
    )
```

```python
import functools

import jax
import jax.numpy as jnp
from jax import lax
from jax.experimental import pallas as pl
from jax.experimental.pallas import tpu as pltpu
from jax.sharding import PartitionSpec as P

HEAD_WIDTH = 128
REACH = 3


def shifted(value, axis, steps):
    count = lax.axis_size(axis)
    first, last = (max(0, -steps), min(count, count - steps))
    return lax.ppermute(value, axis, [(source, source + steps) for source in range(first, last)])


def head_kernel(starts_ref, q_ref, do_ref, k_ref, v_ref, attn_ref, gq_ref, gk_ref, gv_ref, *, scale):
    head = pl.program_id(1)
    q = q_ref[...]
    do = do_ref[...]
    k = k_ref[...]
    v = v_ref[...]
    rows, span = q.shape[0], k.shape[0]
    scores = lax.dot_general(q, k, (((1,), (1,)), ((), ())), preferred_element_type=jnp.float32) * scale
    row = lax.broadcasted_iota(jnp.int32, (rows, span), 0)
    col = lax.broadcasted_iota(jnp.int32, (rows, span), 1)
    visible = (col >= starts_ref[...]) & (col <= row + (span - rows))
    scores = jnp.where(visible, scores, -jnp.inf)
    top = jnp.max(scores, axis=1, keepdims=True)
    total = jnp.sum(jnp.exp(scores - top), axis=1, keepdims=True)
    lse = top + jnp.log(total)
    prob = jnp.exp(scores - lse)
    prob_b = prob.astype(jnp.bfloat16)
    attn = jnp.dot(prob_b, v, preferred_element_type=jnp.float32).astype(jnp.bfloat16)
    attn_ref[...] = attn
    delta = jnp.sum(do.astype(jnp.float32) * attn.astype(jnp.float32), axis=1, keepdims=True)
    dprob = lax.dot_general(do, v, (((1,), (1,)), ((), ())), preferred_element_type=jnp.float32)
    dscore = (prob * (dprob - delta) * scale).astype(jnp.bfloat16)
    gq_ref[...] = jnp.dot(dscore, k, preferred_element_type=jnp.float32).astype(jnp.bfloat16)
    gk = lax.dot_general(dscore, q, (((0,), (0,)), ((), ())), preferred_element_type=jnp.float32)
    gv = lax.dot_general(prob_b, do, (((0,), (0,)), ((), ())), preferred_element_type=jnp.float32)

    @pl.when(head == 0)
    def _():
        gk_ref[...] = gk
        gv_ref[...] = gv

    @pl.when(head > 0)
    def _():
        gk_ref[...] += gk
        gv_ref[...] += gv


def attention_terms(rel_starts, queries, dout, window_k, window_v, first_group, group_size):
    rows = queries.shape[0]
    span, width = window_k.shape
    groups = width // HEAD_WIDTH
    scale = HEAD_WIDTH ** (-0.5)
    kernel = functools.partial(head_kernel, scale=scale)
    q_spec = pl.BlockSpec((rows, HEAD_WIDTH), lambda g, h: (0, (first_group + g) * group_size + h))
    out_spec = pl.BlockSpec((rows, HEAD_WIDTH), lambda g, h: (0, g * group_size + h))
    kv_spec = pl.BlockSpec((span, HEAD_WIDTH), lambda g, h: (0, g))
    out_shape = (rows, groups * group_size * HEAD_WIDTH)
    heads = groups * group_size
    cost = pl.CostEstimate(
        flops=heads * 6 * 2 * rows * span * HEAD_WIDTH,
        transcendentals=heads * 2 * rows * span,
        bytes_accessed=heads * 4 * rows * HEAD_WIDTH * 2 + groups * 2 * span * HEAD_WIDTH * 6,
    )
    return pl.pallas_call(
        kernel,
        grid=(groups, group_size),
        in_specs=[
            pl.BlockSpec((rows, 1), lambda g, h: (0, 0)),
            q_spec,
            q_spec,
            kv_spec,
            kv_spec,
        ],
        out_specs=[out_spec, out_spec, kv_spec, kv_spec],
        out_shape=[
            jax.ShapeDtypeStruct(out_shape, jnp.bfloat16),
            jax.ShapeDtypeStruct(out_shape, jnp.bfloat16),
            jax.ShapeDtypeStruct(window_k.shape, jnp.float32),
            jax.ShapeDtypeStruct(window_k.shape, jnp.float32),
        ],
        compiler_params=pltpu.CompilerParams(
            dimension_semantics=("arbitrary", "arbitrary"),
            vmem_limit_bytes=48 * 1024 * 1024,
        ),
        cost_estimate=cost,
    )(rel_starts, queries, dout, window_k, window_v)


def moved(value, steps):
    count = lax.axis_size("ctx")
    return lax.ppermute(value, "ctx", [(d, d + steps) for d in range(count) if 0 <= d + steps < count])


def earlier_blocks(own):
    two_back = moved(own, 2)
    pair = moved(jnp.stack([own, two_back]), 1)
    return pair[1], two_back, pair[0]


def returned_terms(terms, rows):
    piece = [terms[:, index * rows : (index + 1) * rows] for index in range(REACH + 1)]
    pair = moved(jnp.stack([piece[2], piece[0]]).astype(jnp.bfloat16), -1)
    gathered = piece[1] + pair[1].astype(jnp.float32)
    far = moved(gathered.astype(jnp.bfloat16), -2)
    total = piece[3] + pair[0].astype(jnp.float32) + far.astype(jnp.float32)
    return total.astype(jnp.bfloat16)


def local(queries, keys, values, output_cotangent, doc_start):
    local_tokens = queries.shape[1]
    heads_kv = keys.shape[2] // HEAD_WIDTH
    group_size = queries.shape[2] // keys.shape[2]
    position = lax.axis_index("ctx")
    leading_entry = position * local_tokens
    window_base = leading_entry - REACH * local_tokens
    rel_starts = (doc_start[0] - window_base).astype(jnp.int32)[:, None]
    chunks = [(0, 1), (1, heads_kv - 2), (heads_kv - 1, 1)]
    attn_parts, dq_parts, kv_parts = [], [], []
    previous_window = None
    for index, (first_group, groups) in enumerate(chunks):
        columns = slice(first_group * HEAD_WIDTH, (first_group + groups) * HEAD_WIDTH)
        own_block = jnp.stack([keys[0][:, columns], values[0][:, columns]])
        if previous_window is not None:
            own_block, _ = lax.optimization_barrier((own_block, previous_window))
        three_back, two_back, one_back = earlier_blocks(own_block)
        window = jnp.concatenate([three_back, two_back, one_back, own_block], axis=1)
        previous_window = window
        attn, grad_q, grad_k, grad_v = attention_terms(
            rel_starts,
            queries[0],
            output_cotangent[0],
            window[0],
            window[1],
            first_group,
            group_size,
        )
        attn_parts.append(attn)
        dq_parts.append(shifted(grad_q[None], "section", -1))
        terms = jnp.stack([grad_k, grad_v])
        if index > 0:
            terms, _ = lax.optimization_barrier((terms, dq_parts[-2]))
        kv_grads = returned_terms(terms, local_tokens)
        kv_parts.append(shifted(kv_grads[None], "section", -1))
    attn = jnp.concatenate(attn_parts, axis=1)
    handed_dq = jnp.concatenate(dq_parts, axis=2)
    handed_kv = jnp.concatenate(kv_parts, axis=3)
    return (attn[None], handed_dq, handed_kv)


def solution(mesh):
    return jax.shard_map(
        local,
        mesh=mesh,
        in_specs=(
            P("section", "ctx", None),
            P("section", "ctx", None),
            P("section", "ctx", None),
            P("section", "ctx", None),
            P("section", "ctx"),
        ),
        out_specs=(
            P("section", "ctx", None),
            P("section", "ctx", None),
            P("section", None, "ctx", None),
        ),
        check_vma=False,
    )
```

```python
import functools

import jax
import jax.numpy as jnp
from jax import lax
from jax.experimental import pallas as pl
from jax.experimental.pallas import tpu as pltpu
from jax.sharding import PartitionSpec as P

HEAD_WIDTH = 128
REACH = 3


def shifted(value, axis, steps):
    count = lax.axis_size(axis)
    first, last = (max(0, -steps), min(count, count - steps))
    return lax.ppermute(value, axis, [(source, source + steps) for source in range(first, last)])


def head_kernel(starts_ref, q_ref, do_ref, k_ref, v_ref, attn_ref, gq_ref, gk_ref, gv_ref, *, scale):
    head = pl.program_id(1)
    q = q_ref[...]
    do = do_ref[...]
    k = k_ref[...]
    v = v_ref[...]
    rows, span = q.shape[0], k.shape[0]
    scores = lax.dot_general(q, k, (((1,), (1,)), ((), ())), preferred_element_type=jnp.float32) * scale
    row = lax.broadcasted_iota(jnp.int32, (rows, span), 0)
    col = lax.broadcasted_iota(jnp.int32, (rows, span), 1)
    visible = (col >= starts_ref[...]) & (col <= row + (span - rows))
    scores = jnp.where(visible, scores, -jnp.inf)
    top = jnp.max(scores, axis=1, keepdims=True)
    weight = jnp.exp(scores - top)
    total = jnp.sum(weight, axis=1, keepdims=True)
    prob = weight * (1.0 / total)
    prob_b = prob.astype(jnp.bfloat16)
    attn = jnp.dot(prob_b, v, preferred_element_type=jnp.float32).astype(jnp.bfloat16)
    attn_ref[...] = attn
    delta = jnp.sum(do.astype(jnp.float32) * attn.astype(jnp.float32), axis=1, keepdims=True)
    dprob = lax.dot_general(do, v, (((1,), (1,)), ((), ())), preferred_element_type=jnp.float32)
    dscore = (prob * (dprob - delta) * scale).astype(jnp.bfloat16)
    gq_ref[...] = jnp.dot(dscore, k, preferred_element_type=jnp.float32).astype(jnp.bfloat16)
    gk = lax.dot_general(dscore, q, (((0,), (0,)), ((), ())), preferred_element_type=jnp.float32)
    gv = lax.dot_general(prob_b, do, (((0,), (0,)), ((), ())), preferred_element_type=jnp.float32)

    @pl.when(head == 0)
    def _():
        gk_ref[...] = gk
        gv_ref[...] = gv

    @pl.when(head > 0)
    def _():
        gk_ref[...] += gk
        gv_ref[...] += gv


def attention_terms(rel_starts, queries, dout, window_k, window_v, first_group, group_size):
    rows = queries.shape[0]
    span, width = window_k.shape
    groups = width // HEAD_WIDTH
    scale = HEAD_WIDTH ** (-0.5)
    kernel = functools.partial(head_kernel, scale=scale)
    q_spec = pl.BlockSpec((rows, HEAD_WIDTH), lambda g, h: (0, (first_group + g) * group_size + h))
    out_spec = pl.BlockSpec((rows, HEAD_WIDTH), lambda g, h: (0, g * group_size + h))
    kv_spec = pl.BlockSpec((span, HEAD_WIDTH), lambda g, h: (0, g))
    out_shape = (rows, groups * group_size * HEAD_WIDTH)
    heads = groups * group_size
    cost = pl.CostEstimate(
        flops=heads * 6 * 2 * rows * span * HEAD_WIDTH,
        transcendentals=heads * 2 * rows * span,
        bytes_accessed=heads * 4 * rows * HEAD_WIDTH * 2 + groups * 2 * span * HEAD_WIDTH * 6,
    )
    return pl.pallas_call(
        kernel,
        grid=(groups, group_size),
        in_specs=[
            pl.BlockSpec((rows, 1), lambda g, h: (0, 0)),
            q_spec,
            q_spec,
            kv_spec,
            kv_spec,
        ],
        out_specs=[out_spec, out_spec, kv_spec, kv_spec],
        out_shape=[
            jax.ShapeDtypeStruct(out_shape, jnp.bfloat16),
            jax.ShapeDtypeStruct(out_shape, jnp.bfloat16),
            jax.ShapeDtypeStruct(window_k.shape, jnp.float32),
            jax.ShapeDtypeStruct(window_k.shape, jnp.float32),
        ],
        compiler_params=pltpu.CompilerParams(
            dimension_semantics=("arbitrary", "arbitrary"),
            vmem_limit_bytes=48 * 1024 * 1024,
        ),
        cost_estimate=cost,
    )(rel_starts, queries, dout, window_k, window_v)


def moved(value, steps):
    count = lax.axis_size("ctx")
    return lax.ppermute(value, "ctx", [(d, d + steps) for d in range(count) if 0 <= d + steps < count])


def earlier_blocks(own):
    two_back = moved(own, 2)
    pair = moved(jnp.stack([own, two_back]), 1)
    return pair[1], two_back, pair[0]


def returned_terms(terms, rows):
    piece = [terms[:, index * rows : (index + 1) * rows] for index in range(REACH + 1)]
    pair = moved(jnp.stack([piece[2], piece[0]]).astype(jnp.bfloat16), -1)
    gathered = piece[1] + pair[1].astype(jnp.float32)
    far = moved(gathered.astype(jnp.bfloat16), -2)
    total = piece[3] + pair[0].astype(jnp.float32) + far.astype(jnp.float32)
    return total.astype(jnp.bfloat16)


def local(queries, keys, values, output_cotangent, doc_start):
    local_tokens = queries.shape[1]
    heads_kv = keys.shape[2] // HEAD_WIDTH
    group_size = queries.shape[2] // keys.shape[2]
    position = lax.axis_index("ctx")
    leading_entry = position * local_tokens
    window_base = leading_entry - REACH * local_tokens
    rel_starts = (doc_start[0] - window_base).astype(jnp.int32)[:, None]
    halves = 2
    half_groups = heads_kv // halves
    attn_parts, dq_parts, kv_parts = [], [], []
    for half in range(halves):
        columns = slice(half * half_groups * HEAD_WIDTH, (half + 1) * half_groups * HEAD_WIDTH)
        own_block = jnp.stack([keys[0][:, columns], values[0][:, columns]])
        three_back, two_back, one_back = earlier_blocks(own_block)
        window = jnp.concatenate([three_back, two_back, one_back, own_block], axis=1)
        attn, grad_q, grad_k, grad_v = attention_terms(
            rel_starts,
            queries[0],
            output_cotangent[0],
            window[0],
            window[1],
            half * half_groups,
            group_size,
        )
        attn_parts.append(attn)
        dq_parts.append(shifted(grad_q[None], "section", -1))
        terms = jnp.stack([grad_k, grad_v])
        if half > 0:
            terms, _ = lax.optimization_barrier((terms, dq_parts[-2]))
        kv_grads = returned_terms(terms, local_tokens)
        kv_parts.append(shifted(kv_grads[None], "section", -1))
    attn = jnp.concatenate(attn_parts, axis=1)
    handed_dq = jnp.concatenate(dq_parts, axis=2)
    handed_kv = jnp.concatenate(kv_parts, axis=3)
    return (attn[None], handed_dq, handed_kv)


def solution(mesh):
    return jax.shard_map(
        local,
        mesh=mesh,
        in_specs=(
            P("section", "ctx", None),
            P("section", "ctx", None),
            P("section", "ctx", None),
            P("section", "ctx", None),
            P("section", "ctx"),
        ),
        out_specs=(
            P("section", "ctx", None),
            P("section", "ctx", None),
            P("section", None, "ctx", None),
        ),
        check_vma=False,
    )
```

```python
import functools

import jax
import jax.numpy as jnp
from jax import lax
from jax.experimental import pallas as pl
from jax.experimental.pallas import tpu as pltpu
from jax.sharding import PartitionSpec as P

HEAD_WIDTH = 128
REACH = 3


def shifted(value, axis, steps):
    count = lax.axis_size(axis)
    first, last = (max(0, -steps), min(count, count - steps))
    return lax.ppermute(value, axis, [(source, source + steps) for source in range(first, last)])


def head_kernel(starts_ref, q_ref, do_ref, k_ref, v_ref, attn_ref, gq_ref, gk_ref, gv_ref, *, scale):
    head = pl.program_id(1)
    q = q_ref[...]
    do = do_ref[...]
    k = k_ref[...]
    v = v_ref[...]
    rows, span = q.shape[0], k.shape[0]
    scores = lax.dot_general(q, k, (((1,), (1,)), ((), ())), preferred_element_type=jnp.float32) * scale
    row = lax.broadcasted_iota(jnp.int32, (rows, span), 0)
    col = lax.broadcasted_iota(jnp.int32, (rows, span), 1)
    visible = (col >= starts_ref[...]) & (col <= row + (span - rows))
    scores = jnp.where(visible, scores, -jnp.inf)
    top = jnp.max(scores, axis=1, keepdims=True)
    weight = jnp.exp(scores - top)
    total = jnp.sum(weight, axis=1, keepdims=True)
    prob = weight * (1.0 / total)
    prob_b = prob.astype(jnp.bfloat16)
    attn = jnp.dot(prob_b, v, preferred_element_type=jnp.float32).astype(jnp.bfloat16)
    attn_ref[...] = attn
    delta = jnp.sum(do.astype(jnp.float32) * attn.astype(jnp.float32), axis=1, keepdims=True)
    dprob = lax.dot_general(do, v, (((1,), (1,)), ((), ())), preferred_element_type=jnp.float32)
    dscore = (prob * (dprob - delta) * scale).astype(jnp.bfloat16)
    gq_ref[...] = jnp.dot(dscore, k, preferred_element_type=jnp.float32).astype(jnp.bfloat16)
    gk = lax.dot_general(dscore, q, (((0,), (0,)), ((), ())), preferred_element_type=jnp.float32)
    gv = lax.dot_general(prob_b, do, (((0,), (0,)), ((), ())), preferred_element_type=jnp.float32)

    @pl.when(head == 0)
    def _():
        gk_ref[...] = gk
        gv_ref[...] = gv

    @pl.when(head > 0)
    def _():
        gk_ref[...] += gk
        gv_ref[...] += gv


def attention_terms(rel_starts, queries, dout, window_k, window_v, first_group, group_size):
    rows = queries.shape[0]
    span, width = window_k.shape
    groups = width // HEAD_WIDTH
    scale = HEAD_WIDTH ** (-0.5)
    kernel = functools.partial(head_kernel, scale=scale)
    q_spec = pl.BlockSpec((rows, HEAD_WIDTH), lambda g, h: (0, (first_group + g) * group_size + h))
    out_spec = pl.BlockSpec((rows, HEAD_WIDTH), lambda g, h: (0, g * group_size + h))
    kv_spec = pl.BlockSpec((span, HEAD_WIDTH), lambda g, h: (0, g))
    out_shape = (rows, groups * group_size * HEAD_WIDTH)
    heads = groups * group_size
    cost = pl.CostEstimate(
        flops=heads * 6 * 2 * rows * span * HEAD_WIDTH,
        transcendentals=heads * 2 * rows * span,
        bytes_accessed=heads * 4 * rows * HEAD_WIDTH * 2 + groups * 2 * span * HEAD_WIDTH * 6,
    )
    return pl.pallas_call(
        kernel,
        grid=(groups, group_size),
        in_specs=[
            pl.BlockSpec((rows, 1), lambda g, h: (0, 0)),
            q_spec,
            q_spec,
            kv_spec,
            kv_spec,
        ],
        out_specs=[out_spec, out_spec, kv_spec, kv_spec],
        out_shape=[
            jax.ShapeDtypeStruct(out_shape, jnp.bfloat16),
            jax.ShapeDtypeStruct(out_shape, jnp.bfloat16),
            jax.ShapeDtypeStruct(window_k.shape, jnp.float32),
            jax.ShapeDtypeStruct(window_k.shape, jnp.float32),
        ],
        compiler_params=pltpu.CompilerParams(
            dimension_semantics=("arbitrary", "arbitrary"),
            vmem_limit_bytes=48 * 1024 * 1024,
        ),
        cost_estimate=cost,
    )(rel_starts, queries, dout, window_k, window_v)


def moved(value, steps):
    count = lax.axis_size("ctx")
    return lax.ppermute(value, "ctx", [(d, d + steps) for d in range(count) if 0 <= d + steps < count])


def earlier_blocks(own):
    two_back = moved(own, 2)
    pair = moved(jnp.stack([own, two_back]), 1)
    return pair[1], two_back, pair[0]


def returned_terms(terms, rows):
    piece = [terms[:, index * rows : (index + 1) * rows] for index in range(REACH + 1)]
    total = piece[REACH]
    for behind in range(1, REACH + 1):
        sent = moved(piece[REACH - behind].astype(jnp.bfloat16), -behind)
        total = total + sent.astype(jnp.float32)
    return total.astype(jnp.bfloat16)


def local(queries, keys, values, output_cotangent, doc_start):
    local_tokens = queries.shape[1]
    heads_kv = keys.shape[2] // HEAD_WIDTH
    group_size = queries.shape[2] // keys.shape[2]
    position = lax.axis_index("ctx")
    leading_entry = position * local_tokens
    window_base = leading_entry - REACH * local_tokens
    rel_starts = (doc_start[0] - window_base).astype(jnp.int32)[:, None]
    halves = 2
    half_groups = heads_kv // halves
    attn_parts, dq_parts, kv_parts = [], [], []
    for half in range(halves):
        columns = slice(half * half_groups * HEAD_WIDTH, (half + 1) * half_groups * HEAD_WIDTH)
        own_block = jnp.stack([keys[0][:, columns], values[0][:, columns]])
        three_back, two_back, one_back = earlier_blocks(own_block)
        window = jnp.concatenate([three_back, two_back, one_back, own_block], axis=1)
        attn, grad_q, grad_k, grad_v = attention_terms(
            rel_starts,
            queries[0],
            output_cotangent[0],
            window[0],
            window[1],
            half * half_groups,
            group_size,
        )
        attn_parts.append(attn)
        dq_parts.append(shifted(grad_q[None], "section", -1))
        terms = jnp.stack([grad_k, grad_v])
        if half > 0:
            terms, _ = lax.optimization_barrier((terms, dq_parts[-2]))
        kv_grads = returned_terms(terms, local_tokens)
        kv_parts.append(shifted(kv_grads[None], "section", -1))
    attn = jnp.concatenate(attn_parts, axis=1)
    handed_dq = jnp.concatenate(dq_parts, axis=2)
    handed_kv = jnp.concatenate(kv_parts, axis=3)
    return (attn[None], handed_dq, handed_kv)


def solution(mesh):
    return jax.shard_map(
        local,
        mesh=mesh,
        in_specs=(
            P("section", "ctx", None),
            P("section", "ctx", None),
            P("section", "ctx", None),
            P("section", "ctx", None),
            P("section", "ctx"),
        ),
        out_specs=(
            P("section", "ctx", None),
            P("section", "ctx", None),
            P("section", None, "ctx", None),
        ),
        check_vma=False,
    )
```

```python
import functools

import jax
import jax.numpy as jnp
from jax import lax
from jax.experimental import pallas as pl
from jax.experimental.pallas import tpu as pltpu
from jax.sharding import PartitionSpec as P

HEAD_WIDTH = 128
REACH = 3


def shifted(value, axis, steps):
    count = lax.axis_size(axis)
    first, last = (max(0, -steps), min(count, count - steps))
    return lax.ppermute(value, axis, [(source, source + steps) for source in range(first, last)])


def head_kernel(starts_ref, q_ref, do_ref, k_ref, v_ref, attn_ref, gq_ref, gk_ref, gv_ref, *, scale):
    head = pl.program_id(1)
    q = q_ref[...]
    do = do_ref[...]
    k = k_ref[...]
    v = v_ref[...]
    rows, span = q.shape[0], k.shape[0]
    scores = lax.dot_general(q, k, (((1,), (1,)), ((), ())), preferred_element_type=jnp.float32) * scale
    row = lax.broadcasted_iota(jnp.int32, (rows, span), 0)
    col = lax.broadcasted_iota(jnp.int32, (rows, span), 1)
    visible = (col >= starts_ref[...]) & (col <= row + (span - rows))
    scores = jnp.where(visible, scores, -jnp.inf)
    top = jnp.max(scores, axis=1, keepdims=True)
    weight = jnp.exp(scores - top)
    total = jnp.sum(weight, axis=1, keepdims=True)
    prob = weight * (1.0 / total)
    prob_b = prob.astype(jnp.bfloat16)
    attn = jnp.dot(prob_b, v, preferred_element_type=jnp.float32).astype(jnp.bfloat16)
    attn_ref[...] = attn
    delta = jnp.sum(do.astype(jnp.float32) * attn.astype(jnp.float32), axis=1, keepdims=True)
    dprob = lax.dot_general(do, v, (((1,), (1,)), ((), ())), preferred_element_type=jnp.float32)
    dscore = (prob * (dprob - delta) * scale).astype(jnp.bfloat16)
    gq_ref[...] = jnp.dot(dscore, k, preferred_element_type=jnp.float32).astype(jnp.bfloat16)
    gk = lax.dot_general(dscore, q, (((0,), (0,)), ((), ())), preferred_element_type=jnp.float32)
    gv = lax.dot_general(prob_b, do, (((0,), (0,)), ((), ())), preferred_element_type=jnp.float32)

    @pl.when(head == 0)
    def _():
        gk_ref[...] = gk
        gv_ref[...] = gv

    @pl.when(head > 0)
    def _():
        gk_ref[...] += gk
        gv_ref[...] += gv


def attention_terms(rel_starts, queries, dout, window_k, window_v, first_group, group_size):
    rows = queries.shape[0]
    span, width = window_k.shape
    groups = width // HEAD_WIDTH
    scale = HEAD_WIDTH ** (-0.5)
    kernel = functools.partial(head_kernel, scale=scale)
    q_spec = pl.BlockSpec((rows, HEAD_WIDTH), lambda g, h: (0, (first_group + g) * group_size + h))
    out_spec = pl.BlockSpec((rows, HEAD_WIDTH), lambda g, h: (0, g * group_size + h))
    kv_spec = pl.BlockSpec((span, HEAD_WIDTH), lambda g, h: (0, g))
    out_shape = (rows, groups * group_size * HEAD_WIDTH)
    heads = groups * group_size
    cost = pl.CostEstimate(
        flops=heads * 6 * 2 * rows * span * HEAD_WIDTH,
        transcendentals=heads * 2 * rows * span,
        bytes_accessed=heads * 4 * rows * HEAD_WIDTH * 2 + groups * 2 * span * HEAD_WIDTH * 6,
    )
    return pl.pallas_call(
        kernel,
        grid=(groups, group_size),
        in_specs=[
            pl.BlockSpec((rows, 1), lambda g, h: (0, 0)),
            q_spec,
            q_spec,
            kv_spec,
            kv_spec,
        ],
        out_specs=[out_spec, out_spec, kv_spec, kv_spec],
        out_shape=[
            jax.ShapeDtypeStruct(out_shape, jnp.bfloat16),
            jax.ShapeDtypeStruct(out_shape, jnp.bfloat16),
            jax.ShapeDtypeStruct(window_k.shape, jnp.float32),
            jax.ShapeDtypeStruct(window_k.shape, jnp.float32),
        ],
        compiler_params=pltpu.CompilerParams(
            dimension_semantics=("arbitrary", "arbitrary"),
            vmem_limit_bytes=48 * 1024 * 1024,
        ),
        cost_estimate=cost,
    )(rel_starts, queries, dout, window_k, window_v)


def moved(value, steps):
    count = lax.axis_size("ctx")
    return lax.ppermute(value, "ctx", [(d, d + steps) for d in range(count) if 0 <= d + steps < count])


def earlier_blocks(own):
    two_back = moved(own, 2)
    pair = moved(jnp.stack([own, two_back]), 1)
    return pair[1], two_back, pair[0]


def returned_terms(terms, rows):
    piece = [terms[:, index * rows : (index + 1) * rows] for index in range(REACH + 1)]
    pair = moved(jnp.stack([piece[2], piece[0]]).astype(jnp.bfloat16), -1)
    gathered = piece[1] + pair[1].astype(jnp.float32)
    far = moved(gathered.astype(jnp.bfloat16), -2)
    total = piece[3] + pair[0].astype(jnp.float32) + far.astype(jnp.float32)
    return total.astype(jnp.bfloat16)


def local(queries, keys, values, output_cotangent, doc_start):
    local_tokens = queries.shape[1]
    heads_kv = keys.shape[2] // HEAD_WIDTH
    group_size = queries.shape[2] // keys.shape[2]
    position = lax.axis_index("ctx")
    leading_entry = position * local_tokens
    window_base = leading_entry - REACH * local_tokens
    rel_starts = (doc_start[0] - window_base).astype(jnp.int32)[:, None]
    halves = 2
    half_groups = heads_kv // halves
    attn_parts, dq_parts, kv_parts = [], [], []
    for half in range(halves):
        columns = slice(half * half_groups * HEAD_WIDTH, (half + 1) * half_groups * HEAD_WIDTH)
        own_block = jnp.stack([keys[0][:, columns], values[0][:, columns]])
        three_back, two_back, one_back = earlier_blocks(own_block)
        window = jnp.concatenate([three_back, two_back, one_back, own_block], axis=1)
        attn, grad_q, grad_k, grad_v = attention_terms(
            rel_starts,
            queries[0],
            output_cotangent[0],
            window[0],
            window[1],
            half * half_groups,
            group_size,
        )
        attn_parts.append(attn)
        dq_parts.append(shifted(grad_q[None], "section", -1))
        terms = jnp.stack([grad_k, grad_v])
        if half > 0:
            terms, _ = lax.optimization_barrier((terms, dq_parts[-2]))
        kv_grads = returned_terms(terms, local_tokens)
        kv_parts.append(kv_grads)
    attn = jnp.concatenate(attn_parts, axis=1)
    handed_dq = jnp.concatenate(dq_parts, axis=2)
    handed_kv = shifted(jnp.concatenate(kv_parts, axis=2)[None], "section", -1)
    return (attn[None], handed_dq, handed_kv)


def solution(mesh):
    return jax.shard_map(
        local,
        mesh=mesh,
        in_specs=(
            P("section", "ctx", None),
            P("section", "ctx", None),
            P("section", "ctx", None),
            P("section", "ctx", None),
            P("section", "ctx"),
        ),
        out_specs=(
            P("section", "ctx", None),
            P("section", "ctx", None),
            P("section", None, "ctx", None),
        ),
        check_vma=False,
    )
```

```python
import functools

import jax
import jax.numpy as jnp
from jax import lax
from jax.experimental import pallas as pl
from jax.experimental.pallas import tpu as pltpu
from jax.sharding import PartitionSpec as P

HEAD_WIDTH = 128
REACH = 3


def shifted(value, axis, steps):
    count = lax.axis_size(axis)
    first, last = (max(0, -steps), min(count, count - steps))
    return lax.ppermute(value, axis, [(source, source + steps) for source in range(first, last)])


def head_kernel(starts_ref, q_ref, do_ref, k_ref, v_ref, attn_ref, gq_ref, gk_ref, gv_ref, *, scale):
    head = pl.program_id(1)
    q = q_ref[...]
    do = do_ref[...]
    k = k_ref[...]
    v = v_ref[...]
    rows, span = q.shape[0], k.shape[0]
    scores = lax.dot_general(q, k, (((1,), (1,)), ((), ())), preferred_element_type=jnp.float32) * scale
    row = lax.broadcasted_iota(jnp.int32, (rows, span), 0)
    col = lax.broadcasted_iota(jnp.int32, (rows, span), 1)
    visible = (col >= starts_ref[...]) & (col <= row + (span - rows))
    scores = jnp.where(visible, scores, -jnp.inf)
    top = jnp.max(scores, axis=1, keepdims=True)
    weight = jnp.exp(scores - top)
    total = jnp.sum(weight, axis=1, keepdims=True)
    prob = weight * (1.0 / total)
    prob_b = prob.astype(jnp.bfloat16)
    attn = jnp.dot(prob_b, v, preferred_element_type=jnp.float32).astype(jnp.bfloat16)
    attn_ref[...] = attn
    delta = jnp.sum(do.astype(jnp.float32) * attn.astype(jnp.float32), axis=1, keepdims=True)
    dprob = lax.dot_general(do, v, (((1,), (1,)), ((), ())), preferred_element_type=jnp.float32)
    dscore = (prob * (dprob - delta) * scale).astype(jnp.bfloat16)
    gq_ref[...] = jnp.dot(dscore, k, preferred_element_type=jnp.float32).astype(jnp.bfloat16)
    gk = lax.dot_general(dscore, q, (((0,), (0,)), ((), ())), preferred_element_type=jnp.float32)
    gv = lax.dot_general(prob_b, do, (((0,), (0,)), ((), ())), preferred_element_type=jnp.float32)

    @pl.when(head == 0)
    def _():
        gk_ref[...] = gk
        gv_ref[...] = gv

    @pl.when(head > 0)
    def _():
        gk_ref[...] += gk
        gv_ref[...] += gv


def attention_terms(rel_starts, queries, dout, window_k, window_v, first_group, group_size):
    rows = queries.shape[0]
    span, width = window_k.shape
    groups = width // HEAD_WIDTH
    scale = HEAD_WIDTH ** (-0.5)
    kernel = functools.partial(head_kernel, scale=scale)
    q_spec = pl.BlockSpec((rows, HEAD_WIDTH), lambda g, h: (0, (first_group + g) * group_size + h))
    out_spec = pl.BlockSpec((rows, HEAD_WIDTH), lambda g, h: (0, g * group_size + h))
    kv_spec = pl.BlockSpec((span, HEAD_WIDTH), lambda g, h: (0, g))
    out_shape = (rows, groups * group_size * HEAD_WIDTH)
    heads = groups * group_size
    cost = pl.CostEstimate(
        flops=heads * 6 * 2 * rows * span * HEAD_WIDTH,
        transcendentals=heads * 2 * rows * span,
        bytes_accessed=heads * 4 * rows * HEAD_WIDTH * 2 + groups * 2 * span * HEAD_WIDTH * 6,
    )
    return pl.pallas_call(
        kernel,
        grid=(groups, group_size),
        in_specs=[
            pl.BlockSpec((rows, 1), lambda g, h: (0, 0)),
            q_spec,
            q_spec,
            kv_spec,
            kv_spec,
        ],
        out_specs=[out_spec, out_spec, kv_spec, kv_spec],
        out_shape=[
            jax.ShapeDtypeStruct(out_shape, jnp.bfloat16),
            jax.ShapeDtypeStruct(out_shape, jnp.bfloat16),
            jax.ShapeDtypeStruct(window_k.shape, jnp.float32),
            jax.ShapeDtypeStruct(window_k.shape, jnp.float32),
        ],
        compiler_params=pltpu.CompilerParams(
            dimension_semantics=("arbitrary", "arbitrary"),
            vmem_limit_bytes=48 * 1024 * 1024,
        ),
        cost_estimate=cost,
    )(rel_starts, queries, dout, window_k, window_v)


def moved(value, steps):
    count = lax.axis_size("ctx")
    return lax.ppermute(value, "ctx", [(d, d + steps) for d in range(count) if 0 <= d + steps < count])


def earlier_blocks(own):
    two_back = moved(own, 2)
    pair = moved(jnp.stack([own, two_back]), 1)
    return pair[1], two_back, pair[0]


def returned_terms(terms, rows, pending):
    piece = [terms[:, index * rows : (index + 1) * rows] for index in range(REACH + 1)]
    pair = moved(jnp.stack([piece[2], piece[0]]).astype(jnp.bfloat16), -1)
    gathered = piece[1] + pair[1].astype(jnp.float32)
    far = moved(gathered.astype(jnp.bfloat16), -2)
    pending.append(far)
    total = piece[3] + pair[0].astype(jnp.float32) + far.astype(jnp.float32)
    return total.astype(jnp.bfloat16)


def local(queries, keys, values, output_cotangent, doc_start):
    local_tokens = queries.shape[1]
    heads_kv = keys.shape[2] // HEAD_WIDTH
    group_size = queries.shape[2] // keys.shape[2]
    position = lax.axis_index("ctx")
    leading_entry = position * local_tokens
    window_base = leading_entry - REACH * local_tokens
    rel_starts = (doc_start[0] - window_base).astype(jnp.int32)[:, None]
    halves = 2
    half_groups = heads_kv // halves
    attn_parts, dq_parts, kv_parts = [], [], []
    pending = []
    for half in range(halves):
        columns = slice(half * half_groups * HEAD_WIDTH, (half + 1) * half_groups * HEAD_WIDTH)
        own_block = jnp.stack([keys[0][:, columns], values[0][:, columns]])
        three_back, two_back, one_back = earlier_blocks(own_block)
        window = jnp.concatenate([three_back, two_back, one_back, own_block], axis=1)
        attn, grad_q, grad_k, grad_v = attention_terms(
            rel_starts,
            queries[0],
            output_cotangent[0],
            window[0],
            window[1],
            half * half_groups,
            group_size,
        )
        attn_parts.append(attn)
        dq_parts.append(shifted(grad_q[None], "section", -1))
        terms = jnp.stack([grad_k, grad_v])
        if half > 0:
            terms, _ = lax.optimization_barrier((terms, [dq_parts[-2]] + pending))
        pending = []
        kv_grads = returned_terms(terms, local_tokens, pending)
        kv_parts.append(shifted(kv_grads[None], "section", -1))
    attn = jnp.concatenate(attn_parts, axis=1)
    handed_dq = jnp.concatenate(dq_parts, axis=2)
    handed_kv = jnp.concatenate(kv_parts, axis=3)
    return (attn[None], handed_dq, handed_kv)


def solution(mesh):
    return jax.shard_map(
        local,
        mesh=mesh,
        in_specs=(
            P("section", "ctx", None),
            P("section", "ctx", None),
            P("section", "ctx", None),
            P("section", "ctx", None),
            P("section", "ctx"),
        ),
        out_specs=(
            P("section", "ctx", None),
            P("section", "ctx", None),
            P("section", None, "ctx", None),
        ),
        check_vma=False,
    )
```

```python
import functools

import jax
import jax.numpy as jnp
from jax import lax
from jax.experimental import pallas as pl
from jax.experimental.pallas import tpu as pltpu
from jax.sharding import PartitionSpec as P

HEAD_WIDTH = 128
REACH = 3


def shifted(value, axis, steps):
    count = lax.axis_size(axis)
    first, last = (max(0, -steps), min(count, count - steps))
    return lax.ppermute(value, axis, [(source, source + steps) for source in range(first, last)])


def head_terms(q, do, k, v, starts, scale):
    rows, span = q.shape[0], k.shape[0]
    scores = lax.dot_general(q, k, (((1,), (1,)), ((), ())), preferred_element_type=jnp.float32) * scale
    row = lax.broadcasted_iota(jnp.int32, (rows, span), 0)
    col = lax.broadcasted_iota(jnp.int32, (rows, span), 1)
    visible = (col >= starts) & (col <= row + (span - rows))
    scores = jnp.where(visible, scores, -jnp.inf)
    top = jnp.max(scores, axis=1, keepdims=True)
    weight = jnp.exp(scores - top)
    total = jnp.sum(weight, axis=1, keepdims=True)
    prob = weight * (1.0 / total)
    prob_b = prob.astype(jnp.bfloat16)
    attn = jnp.dot(prob_b, v, preferred_element_type=jnp.float32).astype(jnp.bfloat16)
    delta = jnp.sum(do.astype(jnp.float32) * attn.astype(jnp.float32), axis=1, keepdims=True)
    dprob = lax.dot_general(do, v, (((1,), (1,)), ((), ())), preferred_element_type=jnp.float32)
    dscore = (prob * (dprob - delta) * scale).astype(jnp.bfloat16)
    grad_q = jnp.dot(dscore, k, preferred_element_type=jnp.float32).astype(jnp.bfloat16)
    gk = lax.dot_general(dscore, q, (((0,), (0,)), ((), ())), preferred_element_type=jnp.float32)
    gv = lax.dot_general(prob_b, do, (((0,), (0,)), ((), ())), preferred_element_type=jnp.float32)
    return attn, grad_q, gk, gv


def group_kernel(starts_ref, q_ref, do_ref, k_ref, v_ref, attn_ref, gq_ref, gk_ref, gv_ref, *, scale, heads):
    k = k_ref[...]
    v = v_ref[...]
    starts = starts_ref[...]
    gk_sum, gv_sum = None, None
    for head in range(heads):
        columns = pl.ds(head * HEAD_WIDTH, HEAD_WIDTH)
        attn, grad_q, gk, gv = head_terms(q_ref[:, columns], do_ref[:, columns], k, v, starts, scale)
        attn_ref[:, columns] = attn
        gq_ref[:, columns] = grad_q
        gk_sum = gk if gk_sum is None else gk_sum + gk
        gv_sum = gv if gv_sum is None else gv_sum + gv
    gk_ref[...] = gk_sum
    gv_ref[...] = gv_sum


def attention_terms(rel_starts, queries, dout, window_k, window_v, first_group, group_size):
    rows = queries.shape[0]
    span, width = window_k.shape
    groups = width // HEAD_WIDTH
    scale = HEAD_WIDTH ** (-0.5)
    kernel = functools.partial(group_kernel, scale=scale, heads=group_size)
    group_width = group_size * HEAD_WIDTH
    q_spec = pl.BlockSpec((rows, group_width), lambda g: (0, first_group + g))
    out_spec = pl.BlockSpec((rows, group_width), lambda g: (0, g))
    kv_spec = pl.BlockSpec((span, HEAD_WIDTH), lambda g: (0, g))
    out_shape = (rows, groups * group_width)
    heads = groups * group_size
    cost = pl.CostEstimate(
        flops=heads * 6 * 2 * rows * span * HEAD_WIDTH,
        transcendentals=heads * 2 * rows * span,
        bytes_accessed=heads * 4 * rows * HEAD_WIDTH * 2 + groups * 2 * span * HEAD_WIDTH * 6,
    )
    return pl.pallas_call(
        kernel,
        grid=(groups,),
        in_specs=[
            pl.BlockSpec((rows, 1), lambda g: (0, 0)),
            q_spec,
            q_spec,
            kv_spec,
            kv_spec,
        ],
        out_specs=[out_spec, out_spec, kv_spec, kv_spec],
        out_shape=[
            jax.ShapeDtypeStruct(out_shape, jnp.bfloat16),
            jax.ShapeDtypeStruct(out_shape, jnp.bfloat16),
            jax.ShapeDtypeStruct(window_k.shape, jnp.float32),
            jax.ShapeDtypeStruct(window_k.shape, jnp.float32),
        ],
        compiler_params=pltpu.CompilerParams(
            dimension_semantics=("arbitrary",),
            vmem_limit_bytes=48 * 1024 * 1024,
        ),
        cost_estimate=cost,
    )(rel_starts, queries, dout, window_k, window_v)


def moved(value, steps):
    count = lax.axis_size("ctx")
    return lax.ppermute(value, "ctx", [(d, d + steps) for d in range(count) if 0 <= d + steps < count])


def earlier_blocks(own):
    two_back = moved(own, 2)
    pair = moved(jnp.stack([own, two_back]), 1)
    return pair[1], two_back, pair[0]


def returned_terms(terms, rows):
    piece = [terms[:, index * rows : (index + 1) * rows] for index in range(REACH + 1)]
    pair = moved(jnp.stack([piece[2], piece[0]]).astype(jnp.bfloat16), -1)
    gathered = piece[1] + pair[1].astype(jnp.float32)
    far = moved(gathered.astype(jnp.bfloat16), -2)
    total = piece[3] + pair[0].astype(jnp.float32) + far.astype(jnp.float32)
    return total.astype(jnp.bfloat16)


def local(queries, keys, values, output_cotangent, doc_start):
    local_tokens = queries.shape[1]
    heads_kv = keys.shape[2] // HEAD_WIDTH
    group_size = queries.shape[2] // keys.shape[2]
    position = lax.axis_index("ctx")
    leading_entry = position * local_tokens
    window_base = leading_entry - REACH * local_tokens
    rel_starts = (doc_start[0] - window_base).astype(jnp.int32)[:, None]
    halves = 2
    half_groups = heads_kv // halves
    attn_parts, dq_parts, kv_parts = [], [], []
    for half in range(halves):
        columns = slice(half * half_groups * HEAD_WIDTH, (half + 1) * half_groups * HEAD_WIDTH)
        own_block = jnp.stack([keys[0][:, columns], values[0][:, columns]])
        three_back, two_back, one_back = earlier_blocks(own_block)
        window = jnp.concatenate([three_back, two_back, one_back, own_block], axis=1)
        attn, grad_q, grad_k, grad_v = attention_terms(
            rel_starts,
            queries[0],
            output_cotangent[0],
            window[0],
            window[1],
            half * half_groups,
            group_size,
        )
        attn_parts.append(attn)
        dq_parts.append(shifted(grad_q[None], "section", -1))
        terms = jnp.stack([grad_k, grad_v])
        if half > 0:
            terms, _ = lax.optimization_barrier((terms, dq_parts[-2]))
        kv_grads = returned_terms(terms, local_tokens)
        kv_parts.append(shifted(kv_grads[None], "section", -1))
    attn = jnp.concatenate(attn_parts, axis=1)
    handed_dq = jnp.concatenate(dq_parts, axis=2)
    handed_kv = jnp.concatenate(kv_parts, axis=3)
    return (attn[None], handed_dq, handed_kv)


def solution(mesh):
    return jax.shard_map(
        local,
        mesh=mesh,
        in_specs=(
            P("section", "ctx", None),
            P("section", "ctx", None),
            P("section", "ctx", None),
            P("section", "ctx", None),
            P("section", "ctx"),
        ),
        out_specs=(
            P("section", "ctx", None),
            P("section", "ctx", None),
            P("section", None, "ctx", None),
        ),
        check_vma=False,
    )
```

```python
import functools

import jax
import jax.numpy as jnp
from jax import lax
from jax.experimental import pallas as pl
from jax.experimental.pallas import tpu as pltpu
from jax.sharding import PartitionSpec as P

HEAD_WIDTH = 128
REACH = 3


def shifted(value, axis, steps):
    count = lax.axis_size(axis)
    first, last = (max(0, -steps), min(count, count - steps))
    return lax.ppermute(value, axis, [(source, source + steps) for source in range(first, last)])


def head_terms(q, do, k, v, bias, scale):
    scores = lax.dot_general(q, k, (((1,), (1,)), ((), ())), preferred_element_type=jnp.float32) * scale
    scores = scores + bias
    top = jnp.max(scores, axis=1, keepdims=True)
    weight = jnp.exp(scores - top)
    total = jnp.sum(weight, axis=1, keepdims=True)
    prob = weight * (1.0 / total)
    prob_b = prob.astype(jnp.bfloat16)
    attn = jnp.dot(prob_b, v, preferred_element_type=jnp.float32).astype(jnp.bfloat16)
    delta = jnp.sum(do.astype(jnp.float32) * attn.astype(jnp.float32), axis=1, keepdims=True)
    dprob = lax.dot_general(do, v, (((1,), (1,)), ((), ())), preferred_element_type=jnp.float32)
    dscore = (prob * (dprob - delta) * scale).astype(jnp.bfloat16)
    grad_q = jnp.dot(dscore, k, preferred_element_type=jnp.float32).astype(jnp.bfloat16)
    gk = lax.dot_general(dscore, q, (((0,), (0,)), ((), ())), preferred_element_type=jnp.float32)
    gv = lax.dot_general(prob_b, do, (((0,), (0,)), ((), ())), preferred_element_type=jnp.float32)
    return attn, grad_q, gk, gv


def group_kernel(starts_ref, q_ref, do_ref, k_ref, v_ref, attn_ref, gq_ref, gk_ref, gv_ref, *, scale, heads):
    k = k_ref[...]
    v = v_ref[...]
    rows, span = q_ref.shape[0], k.shape[0]
    row = lax.broadcasted_iota(jnp.int32, (rows, span), 0)
    col = lax.broadcasted_iota(jnp.int32, (rows, span), 1)
    visible = (col >= starts_ref[...]) & (col <= row + (span - rows))
    bias = jnp.where(visible, 0.0, -jnp.inf).astype(jnp.float32)
    gk_sum, gv_sum = None, None
    for head in range(heads):
        columns = pl.ds(head * HEAD_WIDTH, HEAD_WIDTH)
        attn, grad_q, gk, gv = head_terms(q_ref[:, columns], do_ref[:, columns], k, v, bias, scale)
        attn_ref[:, columns] = attn
        gq_ref[:, columns] = grad_q
        gk_sum = gk if gk_sum is None else gk_sum + gk
        gv_sum = gv if gv_sum is None else gv_sum + gv
    gk_ref[...] = gk_sum
    gv_ref[...] = gv_sum


def attention_terms(rel_starts, queries, dout, window_k, window_v, first_group, group_size):
    rows = queries.shape[0]
    span, width = window_k.shape
    groups = width // HEAD_WIDTH
    scale = HEAD_WIDTH ** (-0.5)
    kernel = functools.partial(group_kernel, scale=scale, heads=group_size)
    group_width = group_size * HEAD_WIDTH
    q_spec = pl.BlockSpec((rows, group_width), lambda g: (0, first_group + g))
    out_spec = pl.BlockSpec((rows, group_width), lambda g: (0, g))
    kv_spec = pl.BlockSpec((span, HEAD_WIDTH), lambda g: (0, g))
    out_shape = (rows, groups * group_width)
    heads = groups * group_size
    cost = pl.CostEstimate(
        flops=heads * 6 * 2 * rows * span * HEAD_WIDTH,
        transcendentals=heads * 2 * rows * span,
        bytes_accessed=heads * 4 * rows * HEAD_WIDTH * 2 + groups * 2 * span * HEAD_WIDTH * 6,
    )
    return pl.pallas_call(
        kernel,
        grid=(groups,),
        in_specs=[
            pl.BlockSpec((rows, 1), lambda g: (0, 0)),
            q_spec,
            q_spec,
            kv_spec,
            kv_spec,
        ],
        out_specs=[out_spec, out_spec, kv_spec, kv_spec],
        out_shape=[
            jax.ShapeDtypeStruct(out_shape, jnp.bfloat16),
            jax.ShapeDtypeStruct(out_shape, jnp.bfloat16),
            jax.ShapeDtypeStruct(window_k.shape, jnp.float32),
            jax.ShapeDtypeStruct(window_k.shape, jnp.float32),
        ],
        compiler_params=pltpu.CompilerParams(
            dimension_semantics=("arbitrary",),
            vmem_limit_bytes=48 * 1024 * 1024,
        ),
        cost_estimate=cost,
    )(rel_starts, queries, dout, window_k, window_v)


def moved(value, steps):
    count = lax.axis_size("ctx")
    return lax.ppermute(value, "ctx", [(d, d + steps) for d in range(count) if 0 <= d + steps < count])


def earlier_blocks(own):
    two_back = moved(own, 2)
    pair = moved(jnp.stack([own, two_back]), 1)
    return pair[1], two_back, pair[0]


def returned_terms(terms, rows):
    piece = [terms[:, index * rows : (index + 1) * rows] for index in range(REACH + 1)]
    pair = moved(jnp.stack([piece[2], piece[0]]).astype(jnp.bfloat16), -1)
    gathered = piece[1] + pair[1].astype(jnp.float32)
    far = moved(gathered.astype(jnp.bfloat16), -2)
    total = piece[3] + pair[0].astype(jnp.float32) + far.astype(jnp.float32)
    return total.astype(jnp.bfloat16)


def local(queries, keys, values, output_cotangent, doc_start):
    local_tokens = queries.shape[1]
    heads_kv = keys.shape[2] // HEAD_WIDTH
    group_size = queries.shape[2] // keys.shape[2]
    position = lax.axis_index("ctx")
    leading_entry = position * local_tokens
    window_base = leading_entry - REACH * local_tokens
    rel_starts = (doc_start[0] - window_base).astype(jnp.int32)[:, None]
    halves = 2
    half_groups = heads_kv // halves
    attn_parts, dq_parts, kv_parts = [], [], []
    for half in range(halves):
        columns = slice(half * half_groups * HEAD_WIDTH, (half + 1) * half_groups * HEAD_WIDTH)
        own_block = jnp.stack([keys[0][:, columns], values[0][:, columns]])
        three_back, two_back, one_back = earlier_blocks(own_block)
        window = jnp.concatenate([three_back, two_back, one_back, own_block], axis=1)
        attn, grad_q, grad_k, grad_v = attention_terms(
            rel_starts,
            queries[0],
            output_cotangent[0],
            window[0],
            window[1],
            half * half_groups,
            group_size,
        )
        attn_parts.append(attn)
        dq_parts.append(shifted(grad_q[None], "section", -1))
        terms = jnp.stack([grad_k, grad_v])
        if half > 0:
            terms, _ = lax.optimization_barrier((terms, dq_parts[-2]))
        kv_grads = returned_terms(terms, local_tokens)
        kv_parts.append(shifted(kv_grads[None], "section", -1))
    attn = jnp.concatenate(attn_parts, axis=1)
    handed_dq = jnp.concatenate(dq_parts, axis=2)
    handed_kv = jnp.concatenate(kv_parts, axis=3)
    return (attn[None], handed_dq, handed_kv)


def solution(mesh):
    return jax.shard_map(
        local,
        mesh=mesh,
        in_specs=(
            P("section", "ctx", None),
            P("section", "ctx", None),
            P("section", "ctx", None),
            P("section", "ctx", None),
            P("section", "ctx"),
        ),
        out_specs=(
            P("section", "ctx", None),
            P("section", "ctx", None),
            P("section", None, "ctx", None),
        ),
        check_vma=False,
    )
```

```python
import functools

import jax
import jax.numpy as jnp
from jax import lax
from jax.experimental import pallas as pl
from jax.experimental.pallas import tpu as pltpu
from jax.sharding import PartitionSpec as P

HEAD_WIDTH = 128
REACH = 3


def shifted(value, axis, steps):
    count = lax.axis_size(axis)
    first, last = (max(0, -steps), min(count, count - steps))
    return lax.ppermute(value, axis, [(source, source + steps) for source in range(first, last)])


def head_terms(q, do, k, v, bias, scale):
    scores = lax.dot_general(q, k, (((1,), (1,)), ((), ())), preferred_element_type=jnp.float32) * scale
    scores = scores + bias
    top = jnp.max(scores, axis=1, keepdims=True)
    weight = jnp.exp(scores - top)
    total = jnp.sum(weight, axis=1, keepdims=True)
    prob = weight * (1.0 / total)
    prob_b = prob.astype(jnp.bfloat16)
    attn = jnp.dot(prob_b, v, preferred_element_type=jnp.float32).astype(jnp.bfloat16)
    delta = jnp.sum(do.astype(jnp.float32) * attn.astype(jnp.float32), axis=1, keepdims=True)
    dprob = lax.dot_general(do, v, (((1,), (1,)), ((), ())), preferred_element_type=jnp.float32)
    dscore = (prob * (dprob - delta) * scale).astype(jnp.bfloat16)
    grad_q = jnp.dot(dscore, k, preferred_element_type=jnp.float32).astype(jnp.bfloat16)
    gk = lax.dot_general(dscore, q, (((0,), (0,)), ((), ())), preferred_element_type=jnp.float32)
    gv = lax.dot_general(prob_b, do, (((0,), (0,)), ((), ())), preferred_element_type=jnp.float32)
    return attn, grad_q, gk, gv


def group_kernel(starts_ref, q_ref, do_ref, k_ref, v_ref, attn_ref, gq_ref, gk_ref, gv_ref, *, scale, heads):
    k = k_ref[...]
    v = v_ref[...]
    rows, span = q_ref.shape[0], k.shape[0]
    row = lax.broadcasted_iota(jnp.int32, (rows, span), 0)
    col = lax.broadcasted_iota(jnp.int32, (rows, span), 1)
    visible = (col >= starts_ref[...]) & (col <= row + (span - rows))
    bias = jnp.where(visible, 0.0, -jnp.inf).astype(jnp.float32)
    for head in range(heads):
        columns = pl.ds(head * HEAD_WIDTH, HEAD_WIDTH)
        attn, grad_q, gk, gv = head_terms(q_ref[:, columns], do_ref[:, columns], k, v, bias, scale)
        attn_ref[:, columns] = attn
        gq_ref[:, columns] = grad_q
        if head == 0:
            gk_ref[...] = gk
            gv_ref[...] = gv
        else:
            gk_ref[...] += gk
            gv_ref[...] += gv


def attention_terms(rel_starts, queries, dout, window_k, window_v, first_group, group_size):
    rows = queries.shape[0]
    span, width = window_k.shape
    groups = width // HEAD_WIDTH
    scale = HEAD_WIDTH ** (-0.5)
    kernel = functools.partial(group_kernel, scale=scale, heads=group_size)
    group_width = group_size * HEAD_WIDTH
    q_spec = pl.BlockSpec((rows, group_width), lambda g: (0, first_group + g))
    out_spec = pl.BlockSpec((rows, group_width), lambda g: (0, g))
    kv_spec = pl.BlockSpec((span, HEAD_WIDTH), lambda g: (0, g))
    out_shape = (rows, groups * group_width)
    heads = groups * group_size
    cost = pl.CostEstimate(
        flops=heads * 6 * 2 * rows * span * HEAD_WIDTH,
        transcendentals=heads * 2 * rows * span,
        bytes_accessed=heads * 4 * rows * HEAD_WIDTH * 2 + groups * 2 * span * HEAD_WIDTH * 6,
    )
    return pl.pallas_call(
        kernel,
        grid=(groups,),
        in_specs=[
            pl.BlockSpec((rows, 1), lambda g: (0, 0)),
            q_spec,
            q_spec,
            kv_spec,
            kv_spec,
        ],
        out_specs=[out_spec, out_spec, kv_spec, kv_spec],
        out_shape=[
            jax.ShapeDtypeStruct(out_shape, jnp.bfloat16),
            jax.ShapeDtypeStruct(out_shape, jnp.bfloat16),
            jax.ShapeDtypeStruct(window_k.shape, jnp.float32),
            jax.ShapeDtypeStruct(window_k.shape, jnp.float32),
        ],
        compiler_params=pltpu.CompilerParams(
            dimension_semantics=("arbitrary",),
            vmem_limit_bytes=48 * 1024 * 1024,
        ),
        cost_estimate=cost,
    )(rel_starts, queries, dout, window_k, window_v)


def moved(value, steps):
    count = lax.axis_size("ctx")
    return lax.ppermute(value, "ctx", [(d, d + steps) for d in range(count) if 0 <= d + steps < count])


def earlier_blocks(own):
    two_back = moved(own, 2)
    pair = moved(jnp.stack([own, two_back]), 1)
    return pair[1], two_back, pair[0]


def returned_terms(terms, rows):
    piece = [terms[:, index * rows : (index + 1) * rows] for index in range(REACH + 1)]
    pair = moved(jnp.stack([piece[2], piece[0]]).astype(jnp.bfloat16), -1)
    gathered = piece[1] + pair[1].astype(jnp.float32)
    far = moved(gathered.astype(jnp.bfloat16), -2)
    total = piece[3] + pair[0].astype(jnp.float32) + far.astype(jnp.float32)
    return total.astype(jnp.bfloat16)


def local(queries, keys, values, output_cotangent, doc_start):
    local_tokens = queries.shape[1]
    heads_kv = keys.shape[2] // HEAD_WIDTH
    group_size = queries.shape[2] // keys.shape[2]
    position = lax.axis_index("ctx")
    leading_entry = position * local_tokens
    window_base = leading_entry - REACH * local_tokens
    rel_starts = (doc_start[0] - window_base).astype(jnp.int32)[:, None]
    halves = 2
    half_groups = heads_kv // halves
    attn_parts, dq_parts, kv_parts = [], [], []
    for half in range(halves):
        columns = slice(half * half_groups * HEAD_WIDTH, (half + 1) * half_groups * HEAD_WIDTH)
        own_block = jnp.stack([keys[0][:, columns], values[0][:, columns]])
        three_back, two_back, one_back = earlier_blocks(own_block)
        window = jnp.concatenate([three_back, two_back, one_back, own_block], axis=1)
        attn, grad_q, grad_k, grad_v = attention_terms(
            rel_starts,
            queries[0],
            output_cotangent[0],
            window[0],
            window[1],
            half * half_groups,
            group_size,
        )
        attn_parts.append(attn)
        dq_parts.append(shifted(grad_q[None], "section", -1))
        terms = jnp.stack([grad_k, grad_v])
        if half > 0:
            terms, _ = lax.optimization_barrier((terms, dq_parts[-2]))
        kv_grads = returned_terms(terms, local_tokens)
        kv_parts.append(shifted(kv_grads[None], "section", -1))
    attn = jnp.concatenate(attn_parts, axis=1)
    handed_dq = jnp.concatenate(dq_parts, axis=2)
    handed_kv = jnp.concatenate(kv_parts, axis=3)
    return (attn[None], handed_dq, handed_kv)


def solution(mesh):
    return jax.shard_map(
        local,
        mesh=mesh,
        in_specs=(
            P("section", "ctx", None),
            P("section", "ctx", None),
            P("section", "ctx", None),
            P("section", "ctx", None),
            P("section", "ctx"),
        ),
        out_specs=(
            P("section", "ctx", None),
            P("section", "ctx", None),
            P("section", None, "ctx", None),
        ),
        check_vma=False,
    )
```
